512 devices in a mesh: row: 32 (over z, core), col: 16 (over y, x).
Axes of the slice: x: 4, y: 4, z: 16, core: 2. Of those that a mesh axis runs over, the one named last changes fastest.
Arguments:
- tokens: bfloat16 [512, 8192], P('row', 'col'), may hold values from -6 to 6
- out_grad: bfloat16 [512, 8192], P('row', 'col'), may hold values from -1.5 to 1.5
- gate_weight: bfloat16 [8192, 16384], P('col', 'row'), may hold values from -0.0625 to 0.0625
- up_weight: bfloat16 [8192, 16384], P('col', 'row'), may hold values from -0.0625 to 0.0625
- down_weight: bfloat16 [16384, 8192], P('row', 'col'), may hold values from -0.046875 to 0.046875
Outputs:
- input_grad: bfloat16 [512, 8192], P('row', 'col')
- gate_weight_grad: bfloat16 [8192, 16384], P('col', 'row')
- up_weight_grad: bfloat16 [8192, 16384], P('col', 'row')
- down_weight_grad: bfloat16 [16384, 8192], P('row', 'col')
The draws below stay inside these ranges and needn't reach their ends.
All inputs are finite; a program needn't handle non-finite values.
Results may differ from the reference program's by a relative error of at most 0.005.
Values may be sent and summed in bfloat16 or wider, within the bound.
No kernel may reach another device: no remote copies, remote signals or barrier semaphores. Data moves between devices by JAX's collectives and lax.ppermute only.
A program may use at most 64 MiB of HBM per device.

```python
import jax
import jax.numpy as jnp
from jax import lax

D = 8192
FF = 16384
TOKENS = 512


def block_scale(key, extent, shards, low, top_value):
    gain, own = 1.0, jax.random.fold_in(key, 6)
    for axis_at, parts in shards:
        heights = jnp.exp(jax.random.uniform(jax.random.fold_in(own, axis_at), (parts,), jnp.float32, low / len(shards), top_value / len(shards)))
        gain = gain * jnp.repeat(heights, extent[axis_at] // parts).reshape([-1 if axis == axis_at else 1 for axis in range(len(extent))])
    return gain


def centred(rng, extent, scale, reach, cuts=(), kind=jnp.bfloat16):
    level = block_scale(rng, extent, cuts, -0.22, 0.18) if cuts else 1.0
    values = jax.random.normal(rng, extent, jnp.float32) * scale * level
    return jnp.minimum(jnp.maximum(values, -reach), reach).astype(kind)


def setup_inputs(seed: int = 0) -> dict:
    splits = jax.random.split(jax.random.key(seed), 6)
    return {
        "tokens": centred(splits[0], (TOKENS, D), 1.0, 6.0, ((0, 32), (1, 16))),
        "out_grad": centred(splits[1], (TOKENS, D), 0.25, 1.5, ((0, 32), (1, 16))),
        "gate_weight": centred(splits[2], (D, FF), D ** -0.5, 0.0625, ((0, 16), (1, 32))),
        "up_weight": centred(splits[3], (D, FF), D ** -0.5, 0.0625, ((0, 16), (1, 32))),
        "down_weight": centred(splits[4], (FF, D), FF ** -0.5, 0.046875, ((0, 32), (1, 16))),
    }


def reference(tokens, out_grad, gate_weight, up_weight, down_weight):
    gate = jnp.dot(tokens, gate_weight, preferred_element_type=jnp.float32)
    up = jnp.dot(tokens, up_weight, preferred_element_type=jnp.float32)
    hidden_grad = lax.dot_general(out_grad, down_weight, (((1,), (1,)), ((), ())), preferred_element_type=jnp.float32)
    sig = jax.nn.sigmoid(gate)
    act = gate * sig
    hidden = (act * up).astype(jnp.bfloat16)
    gate_grad = (hidden_grad * up * sig * (1.0 + gate * (1.0 - sig))).astype(jnp.bfloat16)
    up_grad = (hidden_grad * act).astype(jnp.bfloat16)
    contract_rows = (((0,), (0,)), ((), ()))
    gate_weight_grad = lax.dot_general(tokens, gate_grad, contract_rows, preferred_element_type=jnp.float32).astype(jnp.bfloat16)
    up_weight_grad = lax.dot_general(tokens, up_grad, contract_rows, preferred_element_type=jnp.float32).astype(jnp.bfloat16)
    down_weight_grad = lax.dot_general(hidden, out_grad, contract_rows, preferred_element_type=jnp.float32).astype(jnp.bfloat16)
    contract_cols = (((1,), (1,)), ((), ()))
    input_grad = lax.dot_general(gate_grad, gate_weight, contract_cols, preferred_element_type=jnp.float32)
    input_grad = input_grad + lax.dot_general(up_grad, up_weight, contract_cols, preferred_element_type=jnp.float32)
    return (input_grad.astype(jnp.bfloat16), gate_weight_grad, up_weight_grad, down_weight_grad)
```

```python
import jax
import jax.numpy as jnp
from jax import lax
from jax.sharding import PartitionSpec as P


def pointwise(gate, up, hidden_grad):
    sig = jax.nn.sigmoid(gate)
    act = gate * sig
    hidden = (act * up).astype(jnp.bfloat16)
    gate_grad = (hidden_grad * up * sig * (1.0 + gate * (1.0 - sig))).astype(jnp.bfloat16)
    up_grad = (hidden_grad * act).astype(jnp.bfloat16)
    return (hidden, gate_grad, up_grad)


def body(tokens, out_grad, gate_weight, up_weight, down_weight):
    n_col = lax.psum(1, "col")
    n_row = lax.psum(1, "row")
    rows_all = lax.all_gather(tokens, "row", axis=0, tiled=True)
    grads_all = lax.all_gather(out_grad, "row", axis=0, tiled=True)
    n_tok, width = rows_all.shape
    contract_cols = (((1,), (1,)), ((), ()))
    contract_rows = (((0,), (0,)), ((), ()))
    gate_part = jnp.dot(rows_all, gate_weight, preferred_element_type=jnp.float32)
    up_part = jnp.dot(rows_all, up_weight, preferred_element_type=jnp.float32)
    grad_part = lax.dot_general(
        grads_all, down_weight, contract_cols, preferred_element_type=jnp.float32
    )
    hid = gate_part.shape[1]
    chunk = n_tok // n_col
    parts = jnp.stack([gate_part, up_part, grad_part]).reshape(3, n_col, chunk, hid)
    parts = lax.all_to_all(parts, "col", 1, 1, tiled=True)
    gate, up, hidden_grad = parts.sum(axis=1)
    small = jnp.stack(pointwise(gate, up, hidden_grad))
    spread = jnp.broadcast_to(small[None], (n_col,) + small.shape)
    spread = lax.all_to_all(spread, "col", 0, 0, tiled=True)
    spread = spread.transpose(1, 0, 2, 3).reshape(3, n_tok, hid)
    hidden, gate_grad, up_grad = spread[0], spread[1], spread[2]
    gate_weight_grad = lax.dot_general(
        rows_all, gate_grad, contract_rows, preferred_element_type=jnp.float32
    ).astype(jnp.bfloat16)
    up_weight_grad = lax.dot_general(
        rows_all, up_grad, contract_rows, preferred_element_type=jnp.float32
    ).astype(jnp.bfloat16)
    down_weight_grad = lax.dot_general(
        hidden, grads_all, contract_rows, preferred_element_type=jnp.float32
    ).astype(jnp.bfloat16)
    total = lax.dot_general(
        gate_grad, gate_weight, contract_cols, preferred_element_type=jnp.float32
    ) + lax.dot_general(up_grad, up_weight, contract_cols, preferred_element_type=jnp.float32)
    total = total.reshape(n_row, n_tok // n_row, width)
    input_grad = lax.all_to_all(total, "row", 0, 0, tiled=True).sum(axis=0)
    return (input_grad.astype(jnp.bfloat16), gate_weight_grad, up_weight_grad, down_weight_grad)


def solution(mesh):
    return jax.shard_map(
        body,
        mesh=mesh,
        in_specs=(
            P("row", "col"),
            P("row", "col"),
            P("col", "row"),
            P("col", "row"),
            P("row", "col"),
        ),
        out_specs=(P("row", "col"), P("col", "row"), P("col", "row"), P("row", "col")),
        check_vma=False,
    )
```

```python
import jax
import jax.numpy as jnp
from jax import lax
from jax.sharding import Mesh, PartitionSpec as P

ROW = ("z", "core")


def pointwise(gate, up, hidden_grad):
    sig = jax.nn.sigmoid(gate)
    act = gate * sig
    hidden = (act * up).astype(jnp.bfloat16)
    gate_grad = (hidden_grad * up * sig * (1.0 + gate * (1.0 - sig))).astype(jnp.bfloat16)
    up_grad = (hidden_grad * act).astype(jnp.bfloat16)
    return (hidden, gate_grad, up_grad)


def body(tokens, out_grad, gate_weight, up_weight, down_weight):
    n_col = lax.psum(1, "col")
    n_z = lax.psum(1, "z")
    n_core = lax.psum(1, "core")
    rows_all = lax.all_gather(tokens, ROW, axis=0, tiled=True)
    grads_all = lax.all_gather(out_grad, ROW, axis=0, tiled=True)
    n_tok, width = rows_all.shape
    contract_cols = (((1,), (1,)), ((), ()))
    contract_rows = (((0,), (0,)), ((), ()))
    gate_part = jnp.dot(rows_all, gate_weight, preferred_element_type=jnp.float32)
    up_part = jnp.dot(rows_all, up_weight, preferred_element_type=jnp.float32)
    grad_part = lax.dot_general(
        grads_all, down_weight, contract_cols, preferred_element_type=jnp.float32
    )
    hid = gate_part.shape[1]
    chunk = n_tok // n_col
    parts = jnp.stack([gate_part, up_part, grad_part]).reshape(3, n_col, chunk, hid)
    parts = lax.all_to_all(parts, "col", 1, 1, tiled=True)
    gate, up, hidden_grad = parts.sum(axis=1)
    small = jnp.stack(pointwise(gate, up, hidden_grad))
    spread = jnp.broadcast_to(small[None], (n_col,) + small.shape)
    spread = lax.all_to_all(spread, "col", 0, 0, tiled=True)
    spread = spread.transpose(1, 0, 2, 3).reshape(3, n_tok, hid)
    hidden, gate_grad, up_grad = spread[0], spread[1], spread[2]
    gate_weight_grad = lax.dot_general(
        rows_all, gate_grad, contract_rows, preferred_element_type=jnp.float32
    ).astype(jnp.bfloat16)
    up_weight_grad = lax.dot_general(
        rows_all, up_grad, contract_rows, preferred_element_type=jnp.float32
    ).astype(jnp.bfloat16)
    down_weight_grad = lax.dot_general(
        hidden, grads_all, contract_rows, preferred_element_type=jnp.float32
    ).astype(jnp.bfloat16)
    total = lax.dot_general(
        gate_grad, gate_weight, contract_cols, preferred_element_type=jnp.float32
    ) + lax.dot_general(up_grad, up_weight, contract_cols, preferred_element_type=jnp.float32)
    block = n_tok // (n_z * n_core)
    total = total.reshape(n_z, n_core, block, width).transpose(1, 0, 2, 3)
    total = lax.all_to_all(total, "core", 0, 0, tiled=True).sum(axis=0)
    input_grad = lax.all_to_all(total, "z", 0, 0, tiled=True).sum(axis=0)
    return (input_grad.astype(jnp.bfloat16), gate_weight_grad, up_weight_grad, down_weight_grad)


def solution(mesh):
    n_row, n_col = mesh.shape["row"], mesh.shape["col"]
    split = Mesh(mesh.devices.reshape(n_row // 2, 2, n_col), ("z", "core", "col"))
    return jax.shard_map(
        body,
        mesh=split,
        in_specs=(
            P(ROW, "col"),
            P(ROW, "col"),
            P("col", ROW),
            P("col", ROW),
            P(ROW, "col"),
        ),
        out_specs=(P(ROW, "col"), P("col", ROW), P("col", ROW), P(ROW, "col")),
        check_vma=False,
    )
```

```python
import jax
import jax.numpy as jnp
from jax import lax
from jax.sharding import Mesh, PartitionSpec as P

ROW = ("z", "core")


def pointwise(gate, up, hidden_grad):
    sig = jax.nn.sigmoid(gate)
    act = gate * sig
    hidden = (act * up).astype(jnp.bfloat16)
    gate_grad = (hidden_grad * up * sig * (1.0 + gate * (1.0 - sig))).astype(jnp.bfloat16)
    up_grad = (hidden_grad * act).astype(jnp.bfloat16)
    return (hidden, gate_grad, up_grad)


def gather_rows(tokens, out_grad, n_z, n_core):
    both = jnp.stack([tokens, out_grad])
    both = jnp.broadcast_to(both[None], (n_core,) + both.shape)
    both = lax.all_to_all(both, "core", 0, 0, tiled=True)
    mine = lax.dynamic_index_in_dim(both, lax.axis_index("core"), axis=1, keepdims=False)
    mine = mine.reshape((1,) + (-1,) + mine.shape[2:])
    mine = jnp.broadcast_to(mine, (n_z,) + mine.shape[1:])
    mine = lax.all_to_all(mine, "z", 0, 0, tiled=True)
    mine = mine.reshape((1, -1) + mine.shape[2:])
    mine = jnp.broadcast_to(mine, (n_core,) + mine.shape[1:])
    full = lax.all_to_all(mine, "core", 0, 0, tiled=True)
    return full[0], full[1]


def body(tokens, out_grad, gate_weight, up_weight, down_weight):
    n_col = lax.psum(1, "col")
    n_z = lax.psum(1, "z")
    n_core = lax.psum(1, "core")
    rows_all, grads_all = gather_rows(tokens, out_grad, n_z, n_core)
    n_tok, width = rows_all.shape
    contract_cols = (((1,), (1,)), ((), ()))
    contract_rows = (((0,), (0,)), ((), ()))
    gate_part = jnp.dot(rows_all, gate_weight, preferred_element_type=jnp.float32)
    up_part = jnp.dot(rows_all, up_weight, preferred_element_type=jnp.float32)
    grad_part = lax.dot_general(
        grads_all, down_weight, contract_cols, preferred_element_type=jnp.float32
    )
    hid = gate_part.shape[1]
    chunk = n_tok // n_col
    parts = jnp.stack([gate_part, up_part, grad_part]).reshape(3, n_col, chunk, hid)
    parts = lax.all_to_all(parts, "col", 1, 1, tiled=True)
    gate, up, hidden_grad = parts.sum(axis=1)
    small = jnp.stack(pointwise(gate, up, hidden_grad))
    spread = jnp.broadcast_to(small[None], (n_col,) + small.shape)
    spread = lax.all_to_all(spread, "col", 0, 0, tiled=True)
    spread = spread.transpose(1, 0, 2, 3).reshape(3, n_tok, hid)
    hidden, gate_grad, up_grad = spread[0], spread[1], spread[2]
    gate_weight_grad = lax.dot_general(
        rows_all, gate_grad, contract_rows, preferred_element_type=jnp.float32
    ).astype(jnp.bfloat16)
    up_weight_grad = lax.dot_general(
        rows_all, up_grad, contract_rows, preferred_element_type=jnp.float32
    ).astype(jnp.bfloat16)
    down_weight_grad = lax.dot_general(
        hidden, grads_all, contract_rows, preferred_element_type=jnp.float32
    ).astype(jnp.bfloat16)
    total = lax.dot_general(
        gate_grad, gate_weight, contract_cols, preferred_element_type=jnp.float32
    ) + lax.dot_general(up_grad, up_weight, contract_cols, preferred_element_type=jnp.float32)
    block = n_tok // (n_z * n_core)
    total = total.reshape(n_z, n_core, block, width).transpose(1, 0, 2, 3)
    total = lax.all_to_all(total, "core", 0, 0, tiled=True).sum(axis=0)
    input_grad = lax.all_to_all(total, "z", 0, 0, tiled=True).sum(axis=0)
    return (input_grad.astype(jnp.bfloat16), gate_weight_grad, up_weight_grad, down_weight_grad)


def solution(mesh):
    n_row, n_col = mesh.shape["row"], mesh.shape["col"]
    split = Mesh(mesh.devices.reshape(n_row // 2, 2, n_col), ("z", "core", "col"))
    return jax.shard_map(
        body,
        mesh=split,
        in_specs=(
            P(ROW, "col"),
            P(ROW, "col"),
            P("col", ROW),
            P("col", ROW),
            P(ROW, "col"),
        ),
        out_specs=(P(ROW, "col"), P("col", ROW), P("col", ROW), P(ROW, "col")),
        check_vma=False,
    )
```

```python
import jax
import jax.numpy as jnp
from jax import lax
from jax.sharding import Mesh, PartitionSpec as P

ROW = ("z", "core")


def pointwise(gate, up, hidden_grad):
    sig = jax.nn.sigmoid(gate)
    act = gate * sig
    hidden = (act * up).astype(jnp.bfloat16)
    gate_grad = (hidden_grad * up * sig * (1.0 + gate * (1.0 - sig))).astype(jnp.bfloat16)
    up_grad = (hidden_grad * act).astype(jnp.bfloat16)
    return (hidden, gate_grad, up_grad)


def gather_rows(tokens, out_grad, n_z, n_core):
    both = jnp.stack([tokens, out_grad])
    both = jnp.broadcast_to(both[None], (n_z,) + both.shape)
    both = both.reshape((n_z * n_core,) + tokens.shape)
    mine = lax.all_to_all(both, ROW, 0, 0, tiled=True)
    mine = mine.reshape((1, -1) + tokens.shape[1:])
    mine = jnp.broadcast_to(mine, (n_core,) + mine.shape[1:])
    full = lax.all_to_all(mine, "core", 0, 0, tiled=True)
    return full[0], full[1]


def body(tokens, out_grad, gate_weight, up_weight, down_weight):
    n_col = lax.psum(1, "col")
    n_z = lax.psum(1, "z")
    n_core = lax.psum(1, "core")
    rows_all, grads_all = gather_rows(tokens, out_grad, n_z, n_core)
    n_tok, width = rows_all.shape
    contract_cols = (((1,), (1,)), ((), ()))
    contract_rows = (((0,), (0,)), ((), ()))
    gate_part = jnp.dot(rows_all, gate_weight, preferred_element_type=jnp.float32)
    up_part = jnp.dot(rows_all, up_weight, preferred_element_type=jnp.float32)
    grad_part = lax.dot_general(
        grads_all, down_weight, contract_cols, preferred_element_type=jnp.float32
    )
    hid = gate_part.shape[1]
    chunk = n_tok // n_col
    parts = jnp.stack([gate_part, up_part, grad_part]).reshape(3, n_col, chunk, hid)
    parts = lax.all_to_all(parts, "col", 1, 1, tiled=True)
    gate, up, hidden_grad = parts.sum(axis=1)
    small = jnp.stack(pointwise(gate, up, hidden_grad))
    spread = jnp.broadcast_to(small[None], (n_col,) + small.shape)
    spread = lax.all_to_all(spread, "col", 0, 0, tiled=True)
    spread = spread.transpose(1, 0, 2, 3).reshape(3, n_tok, hid)
    hidden, gate_grad, up_grad = spread[0], spread[1], spread[2]
    gate_weight_grad = lax.dot_general(
        rows_all, gate_grad, contract_rows, preferred_element_type=jnp.float32
    ).astype(jnp.bfloat16)
    up_weight_grad = lax.dot_general(
        rows_all, up_grad, contract_rows, preferred_element_type=jnp.float32
    ).astype(jnp.bfloat16)
    down_weight_grad = lax.dot_general(
        hidden, grads_all, contract_rows, preferred_element_type=jnp.float32
    ).astype(jnp.bfloat16)
    total = lax.dot_general(
        gate_grad, gate_weight, contract_cols, preferred_element_type=jnp.float32
    ) + lax.dot_general(up_grad, up_weight, contract_cols, preferred_element_type=jnp.float32)
    block = n_tok // (n_z * n_core)
    total = total.reshape(n_z, n_core, block, width).transpose(1, 0, 2, 3)
    total = lax.all_to_all(total, "core", 0, 0, tiled=True).sum(axis=0)
    input_grad = lax.all_to_all(total, "z", 0, 0, tiled=True).sum(axis=0)
    return (input_grad.astype(jnp.bfloat16), gate_weight_grad, up_weight_grad, down_weight_grad)


def solution(mesh):
    n_row, n_col = mesh.shape["row"], mesh.shape["col"]
    split = Mesh(mesh.devices.reshape(n_row // 2, 2, n_col), ("z", "core", "col"))
    return jax.shard_map(
        body,
        mesh=split,
        in_specs=(
            P(ROW, "col"),
            P(ROW, "col"),
            P("col", ROW),
            P("col", ROW),
            P(ROW, "col"),
        ),
        out_specs=(P(ROW, "col"), P("col", ROW), P("col", ROW), P(ROW, "col")),
        check_vma=False,
    )
```

```python
import jax
import jax.numpy as jnp
from jax import lax
from jax.sharding import Mesh, PartitionSpec as P

ROW = ("z", "core")


def pointwise(gate, up, hidden_grad):
    sig = jax.nn.sigmoid(gate)
    act = gate * sig
    hidden = (act * up).astype(jnp.bfloat16)
    gate_grad = (hidden_grad * up * sig * (1.0 + gate * (1.0 - sig))).astype(jnp.bfloat16)
    up_grad = (hidden_grad * act).astype(jnp.bfloat16)
    return (hidden, gate_grad, up_grad)


def gather_rows(tokens, out_grad, n_z, n_core):
    both = jnp.stack([tokens, out_grad])
    both = jnp.broadcast_to(both[None], (n_z,) + both.shape)
    both = both.reshape((n_z * n_core,) + tokens.shape)
    mine = lax.all_to_all(both, ROW, 0, 0, tiled=True)
    mine = mine.reshape((1, -1) + tokens.shape[1:])
    mine = jnp.broadcast_to(mine, (n_core,) + mine.shape[1:])
    full = lax.all_to_all(mine, "core", 0, 0, tiled=True)
    return full[0], full[1]


def body(tokens, out_grad, gate_weight, up_weight, down_weight):
    n_col = lax.psum(1, "col")
    n_z = lax.psum(1, "z")
    n_core = lax.psum(1, "core")
    rows_all, grads_all = gather_rows(tokens, out_grad, n_z, n_core)
    n_tok, width = rows_all.shape
    contract_cols = (((1,), (1,)), ((), ()))
    contract_rows = (((0,), (0,)), ((), ()))
    gate_part = jnp.dot(rows_all, gate_weight, preferred_element_type=jnp.float32)
    up_part = jnp.dot(rows_all, up_weight, preferred_element_type=jnp.float32)
    grad_part = lax.dot_general(
        grads_all, down_weight, contract_cols, preferred_element_type=jnp.float32
    )
    hid = gate_part.shape[1]
    chunk = n_tok // n_col
    parts = jnp.concatenate([gate_part, up_part, grad_part], axis=1)
    parts = lax.all_to_all(parts.reshape(n_col, chunk, 3 * hid), "col", 0, 0, tiled=True)
    parts = parts.sum(axis=0)
    gate, up, hidden_grad = parts[:, :hid], parts[:, hid:2 * hid], parts[:, 2 * hid:]
    small = jnp.concatenate(pointwise(gate, up, hidden_grad), axis=1)
    spread = jnp.broadcast_to(small[None], (n_col,) + small.shape)
    spread = lax.all_to_all(spread, "col", 0, 0, tiled=True).reshape(n_tok, 3 * hid)
    hidden, gate_grad, up_grad = spread[:, :hid], spread[:, hid:2 * hid], spread[:, 2 * hid:]
    gate_weight_grad = lax.dot_general(
        rows_all, gate_grad, contract_rows, preferred_element_type=jnp.float32
    ).astype(jnp.bfloat16)
    up_weight_grad = lax.dot_general(
        rows_all, up_grad, contract_rows, preferred_element_type=jnp.float32
    ).astype(jnp.bfloat16)
    down_weight_grad = lax.dot_general(
        hidden, grads_all, contract_rows, preferred_element_type=jnp.float32
    ).astype(jnp.bfloat16)
    total = lax.dot_general(
        gate_grad, gate_weight, contract_cols, preferred_element_type=jnp.float32
    ) + lax.dot_general(up_grad, up_weight, contract_cols, preferred_element_type=jnp.float32)
    block = n_tok // (n_z * n_core)
    total = total.reshape(n_z, n_core, block, width).transpose(1, 0, 2, 3)
    total = lax.all_to_all(total, "core", 0, 0, tiled=True).sum(axis=0)
    input_grad = lax.all_to_all(total, "z", 0, 0, tiled=True).sum(axis=0)
    return (input_grad.astype(jnp.bfloat16), gate_weight_grad, up_weight_grad, down_weight_grad)


def solution(mesh):
    n_row, n_col = mesh.shape["row"], mesh.shape["col"]
    split = Mesh(mesh.devices.reshape(n_row // 2, 2, n_col), ("z", "core", "col"))
    return jax.shard_map(
        body,
        mesh=split,
        in_specs=(
            P(ROW, "col"),
            P(ROW, "col"),
            P("col", ROW),
            P("col", ROW),
            P(ROW, "col"),
        ),
        out_specs=(P(ROW, "col"), P("col", ROW), P("col", ROW), P(ROW, "col")),
        check_vma=False,
    )
```

```python
import jax
import jax.numpy as jnp
from jax import lax
from jax.experimental.layout import Layout, with_layout_constraint
from jax.sharding import Mesh, PartitionSpec as P

ROW = ("z", "core")


def pointwise(gate, up, hidden_grad):
    sig = jax.nn.sigmoid(gate)
    act = gate * sig
    hidden = (act * up).astype(jnp.bfloat16)
    gate_grad = (hidden_grad * up * sig * (1.0 + gate * (1.0 - sig))).astype(jnp.bfloat16)
    up_grad = (hidden_grad * act).astype(jnp.bfloat16)
    return (hidden, gate_grad, up_grad)


def gather_rows(tokens, out_grad, n_z, n_core):
    both = jnp.stack([tokens, out_grad])
    both = jnp.broadcast_to(both[None], (n_z,) + both.shape)
    both = both.reshape((n_z * n_core,) + tokens.shape)
    mine = lax.all_to_all(both, ROW, 0, 0, tiled=True)
    mine = mine.reshape((1, -1) + tokens.shape[1:])
    mine = jnp.broadcast_to(mine, (n_core,) + mine.shape[1:])
    full = lax.all_to_all(mine, "core", 0, 0, tiled=True)
    return full[0], full[1]


def body(tokens, out_grad, gate_weight, up_weight, down_weight):
    n_col = lax.psum(1, "col")
    n_z = lax.psum(1, "z")
    n_core = lax.psum(1, "core")
    rows_all, grads_all = gather_rows(tokens, out_grad, n_z, n_core)
    n_tok, width = rows_all.shape
    contract_cols = (((1,), (1,)), ((), ()))
    contract_rows = (((0,), (0,)), ((), ()))
    gate_part = jnp.dot(rows_all, gate_weight, preferred_element_type=jnp.float32)
    up_part = jnp.dot(rows_all, up_weight, preferred_element_type=jnp.float32)
    grad_part = lax.dot_general(
        grads_all, down_weight, contract_cols, preferred_element_type=jnp.float32
    )
    hid = gate_part.shape[1]
    chunk = n_tok // n_col
    parts = jnp.stack([p.reshape(n_col, chunk, hid) for p in (gate_part, up_part, grad_part)], axis=1)
    parts = with_layout_constraint(parts, Layout(major_to_minor=(0, 1, 2, 3)))
    parts = lax.all_to_all(parts, "col", 0, 0, tiled=True)
    gate, up, hidden_grad = parts.sum(axis=0)
    small = jnp.stack(pointwise(gate, up, hidden_grad))
    spread = jnp.broadcast_to(small[None], (n_col,) + small.shape)
    spread = lax.all_to_all(spread, "col", 0, 0, tiled=True)
    spread = spread.transpose(1, 0, 2, 3).reshape(3, n_tok, hid)
    hidden, gate_grad, up_grad = spread[0], spread[1], spread[2]
    gate_weight_grad = lax.dot_general(
        rows_all, gate_grad, contract_rows, preferred_element_type=jnp.float32
    ).astype(jnp.bfloat16)
    up_weight_grad = lax.dot_general(
        rows_all, up_grad, contract_rows, preferred_element_type=jnp.float32
    ).astype(jnp.bfloat16)
    down_weight_grad = lax.dot_general(
        hidden, grads_all, contract_rows, preferred_element_type=jnp.float32
    ).astype(jnp.bfloat16)
    total = lax.dot_general(
        gate_grad, gate_weight, contract_cols, preferred_element_type=jnp.float32
    ) + lax.dot_general(up_grad, up_weight, contract_cols, preferred_element_type=jnp.float32)
    block = n_tok // (n_z * n_core)
    total = total.reshape(n_z, n_core, block, width).transpose(1, 0, 2, 3)
    total = lax.all_to_all(total, "core", 0, 0, tiled=True).sum(axis=0)
    input_grad = lax.all_to_all(total, "z", 0, 0, tiled=True).sum(axis=0)
    return (input_grad.astype(jnp.bfloat16), gate_weight_grad, up_weight_grad, down_weight_grad)


def solution(mesh):
    n_row, n_col = mesh.shape["row"], mesh.shape["col"]
    split = Mesh(mesh.devices.reshape(n_row // 2, 2, n_col), ("z", "core", "col"))
    return jax.shard_map(
        body,
        mesh=split,
        in_specs=(
            P(ROW, "col"),
            P(ROW, "col"),
            P("col", ROW),
            P("col", ROW),
            P(ROW, "col"),
        ),
        out_specs=(P(ROW, "col"), P("col", ROW), P("col", ROW), P(ROW, "col")),
        check_vma=False,
    )
```

```python
import jax
import jax.numpy as jnp
from jax import lax
from jax.experimental.layout import Layout, with_layout_constraint
from jax.sharding import Mesh, PartitionSpec as P

ROW = ("z", "core")


def pointwise(gate, up, hidden_grad):
    sig = jax.nn.sigmoid(gate)
    act = gate * sig
    hidden = (act * up).astype(jnp.bfloat16)
    gate_grad = (hidden_grad * up * sig * (1.0 + gate * (1.0 - sig))).astype(jnp.bfloat16)
    up_grad = (hidden_grad * act).astype(jnp.bfloat16)
    return (hidden, gate_grad, up_grad)


def gather_rows(tokens, out_grad, n_z, n_core):
    both = jnp.stack([tokens, out_grad])
    both = jnp.broadcast_to(both[None], (n_z,) + both.shape)
    both = both.reshape((n_z * n_core,) + tokens.shape)
    mine = lax.all_to_all(both, ROW, 0, 0, tiled=True)
    mine = mine.reshape((1, -1) + tokens.shape[1:])
    mine = jnp.broadcast_to(mine, (n_core,) + mine.shape[1:])
    full = lax.all_to_all(mine, "core", 0, 0, tiled=True)
    return full[0], full[1]


def body(tokens, out_grad, gate_weight, up_weight, down_weight):
    n_col = lax.psum(1, "col")
    n_z = lax.psum(1, "z")
    n_core = lax.psum(1, "core")
    rows_all, grads_all = gather_rows(tokens, out_grad, n_z, n_core)
    n_tok, width = rows_all.shape
    contract_cols = (((1,), (1,)), ((), ()))
    contract_rows = (((0,), (0,)), ((), ()))
    gate_part = jnp.dot(rows_all, gate_weight, preferred_element_type=jnp.float32)
    up_part = jnp.dot(rows_all, up_weight, preferred_element_type=jnp.float32)
    grad_part = lax.dot_general(
        grads_all, down_weight, contract_cols, preferred_element_type=jnp.float32
    )
    hid = gate_part.shape[1]
    chunk = n_tok // n_col
    parts = jnp.stack([p.reshape(n_col, chunk, hid) for p in (gate_part, up_part, grad_part)], axis=1)
    parts = with_layout_constraint(parts, Layout(major_to_minor=(0, 1, 2, 3)))
    parts = lax.all_to_all(parts, "col", 0, 0, tiled=True)
    groups = parts.reshape((4, n_col // 4) + parts.shape[1:]).sum(axis=1)
    gate, up, hidden_grad = lax.optimization_barrier(groups).sum(axis=0)
    small = jnp.stack(pointwise(gate, up, hidden_grad))
    spread = jnp.broadcast_to(small[None], (n_col,) + small.shape)
    spread = lax.all_to_all(spread, "col", 0, 0, tiled=True)
    spread = spread.transpose(1, 0, 2, 3).reshape(3, n_tok, hid)
    hidden, gate_grad, up_grad = spread[0], spread[1], spread[2]
    gate_weight_grad = lax.dot_general(
        rows_all, gate_grad, contract_rows, preferred_element_type=jnp.float32
    ).astype(jnp.bfloat16)
    up_weight_grad = lax.dot_general(
        rows_all, up_grad, contract_rows, preferred_element_type=jnp.float32
    ).astype(jnp.bfloat16)
    down_weight_grad = lax.dot_general(
        hidden, grads_all, contract_rows, preferred_element_type=jnp.float32
    ).astype(jnp.bfloat16)
    total = lax.dot_general(
        gate_grad, gate_weight, contract_cols, preferred_element_type=jnp.float32
    ) + lax.dot_general(up_grad, up_weight, contract_cols, preferred_element_type=jnp.float32)
    block = n_tok // (n_z * n_core)
    total = total.reshape(n_z, n_core, block, width).transpose(1, 0, 2, 3)
    total = lax.all_to_all(total, "core", 0, 0, tiled=True).sum(axis=0)
    input_grad = lax.all_to_all(total, "z", 0, 0, tiled=True).sum(axis=0)
    return (input_grad.astype(jnp.bfloat16), gate_weight_grad, up_weight_grad, down_weight_grad)


def solution(mesh):
    n_row, n_col = mesh.shape["row"], mesh.shape["col"]
    split = Mesh(mesh.devices.reshape(n_row // 2, 2, n_col), ("z", "core", "col"))
    return jax.shard_map(
        body,
        mesh=split,
        in_specs=(
            P(ROW, "col"),
            P(ROW, "col"),
            P("col", ROW),
            P("col", ROW),
            P(ROW, "col"),
        ),
        out_specs=(P(ROW, "col"), P("col", ROW), P("col", ROW), P(ROW, "col")),
        check_vma=False,
    )
```

```python
import jax
import jax.numpy as jnp
from jax import lax
from jax.experimental.layout import Layout, with_layout_constraint
from jax.sharding import Mesh, PartitionSpec as P

ROW = ("z", "core")


def pointwise(gate, up, hidden_grad):
    sig = jax.nn.sigmoid(gate)
    act = gate * sig
    hidden = (act * up).astype(jnp.bfloat16)
    gate_grad = (hidden_grad * up * sig * (1.0 + gate * (1.0 - sig))).astype(jnp.bfloat16)
    up_grad = (hidden_grad * act).astype(jnp.bfloat16)
    return (hidden, gate_grad, up_grad)


def gather_rows(tokens, out_grad, n_z, n_core):
    both = jnp.stack([tokens, out_grad])
    both = jnp.broadcast_to(both[None], (n_z,) + both.shape)
    both = both.reshape((n_z * n_core,) + tokens.shape)
    mine = lax.all_to_all(both, ROW, 0, 0, tiled=True)
    mine = mine.reshape((1, -1) + tokens.shape[1:])
    mine = jnp.broadcast_to(mine, (n_core,) + mine.shape[1:])
    full = lax.all_to_all(mine, "core", 0, 0, tiled=True)
    return full[0], full[1]


def body(tokens, out_grad, gate_weight, up_weight, down_weight):
    n_col = lax.psum(1, "col")
    n_z = lax.psum(1, "z")
    n_core = lax.psum(1, "core")
    rows_all, grads_all = gather_rows(tokens, out_grad, n_z, n_core)
    n_tok, width = rows_all.shape
    contract_cols = (((1,), (1,)), ((), ()))
    contract_rows = (((0,), (0,)), ((), ()))
    gate_part = jnp.dot(rows_all, gate_weight, preferred_element_type=jnp.float32)
    up_part = jnp.dot(rows_all, up_weight, preferred_element_type=jnp.float32)
    grad_part = lax.dot_general(
        grads_all, down_weight, contract_cols, preferred_element_type=jnp.float32
    )
    hid = gate_part.shape[1]
    chunk = n_tok // n_col
    parts = jnp.stack([p.reshape(n_col, chunk, hid) for p in (gate_part, up_part, grad_part)], axis=1)
    parts = with_layout_constraint(parts, Layout(major_to_minor=(0, 1, 2, 3)))
    parts = lax.all_to_all(parts, "col", 0, 0, tiled=True)
    groups = parts.reshape((4, n_col // 4) + parts.shape[1:]).sum(axis=1)
    gate, up, hidden_grad = lax.optimization_barrier(groups).sum(axis=0)
    small = jnp.stack(pointwise(gate, up, hidden_grad))
    spread = jnp.broadcast_to(small[None], (n_col,) + small.shape)
    spread = lax.all_to_all(spread, "col", 0, 0, tiled=True)
    spread = spread.transpose(1, 0, 2, 3).reshape(3, n_tok, hid)
    hidden, gate_grad, up_grad = spread[0], spread[1], spread[2]
    gate_weight_grad = lax.dot_general(
        rows_all, gate_grad, contract_rows, preferred_element_type=jnp.float32
    ).astype(jnp.bfloat16)
    up_weight_grad = lax.dot_general(
        rows_all, up_grad, contract_rows, preferred_element_type=jnp.float32
    ).astype(jnp.bfloat16)
    down_weight_grad = lax.dot_general(
        hidden, grads_all, contract_rows, preferred_element_type=jnp.float32
    ).astype(jnp.bfloat16)
    total = lax.dot_general(
        gate_grad, gate_weight, contract_cols, preferred_element_type=jnp.float32
    ) + lax.dot_general(up_grad, up_weight, contract_cols, preferred_element_type=jnp.float32)
    block = n_tok // (n_z * n_core)
    total = total.reshape(n_z, n_core, block, width).transpose(1, 0, 2, 3)
    total = lax.all_to_all(total, "core", 0, 0, tiled=True).sum(axis=0)
    total = lax.all_to_all(total, "z", 0, 0, tiled=True)
    total = total.reshape((4, n_z // 4) + total.shape[1:]).sum(axis=1)
    input_grad = lax.optimization_barrier(total).sum(axis=0)
    return (input_grad.astype(jnp.bfloat16), gate_weight_grad, up_weight_grad, down_weight_grad)


def solution(mesh):
    n_row, n_col = mesh.shape["row"], mesh.shape["col"]
    split = Mesh(mesh.devices.reshape(n_row // 2, 2, n_col), ("z", "core", "col"))
    return jax.shard_map(
        body,
        mesh=split,
        in_specs=(
            P(ROW, "col"),
            P(ROW, "col"),
            P("col", ROW),
            P("col", ROW),
            P(ROW, "col"),
        ),
        out_specs=(P(ROW, "col"), P("col", ROW), P("col", ROW), P(ROW, "col")),
        check_vma=False,
    )
```

```python
import jax
import jax.numpy as jnp
from jax import lax
from jax.experimental.layout import Layout, with_layout_constraint
from jax.sharding import Mesh, PartitionSpec as P

ROW = ("z", "core")


def pointwise(gate, up, hidden_grad):
    sig = jax.nn.sigmoid(gate)
    act = gate * sig
    hidden = (act * up).astype(jnp.bfloat16)
    gate_grad = (hidden_grad * up * sig * (1.0 + gate * (1.0 - sig))).astype(jnp.bfloat16)
    up_grad = (hidden_grad * act).astype(jnp.bfloat16)
    return (hidden, gate_grad, up_grad)


def gather_rows(tokens, out_grad, n_z, n_core):
    both = jnp.stack([tokens, out_grad])
    both = jnp.broadcast_to(both[None], (n_z,) + both.shape)
    both = both.reshape((n_z * n_core,) + tokens.shape)
    mine = lax.all_to_all(both, ROW, 0, 0, tiled=True)
    mine = mine.reshape((1, -1) + tokens.shape[1:])
    mine = jnp.broadcast_to(mine, (n_core,) + mine.shape[1:])
    full = lax.all_to_all(mine, "core", 0, 0, tiled=True)
    return full[0], full[1]


def body(tokens, out_grad, gate_weight, up_weight, down_weight):
    n_col = lax.psum(1, "col")
    n_z = lax.psum(1, "z")
    n_core = lax.psum(1, "core")
    rows_all, grads_all = gather_rows(tokens, out_grad, n_z, n_core)
    n_tok, width = rows_all.shape
    contract_cols = (((1,), (1,)), ((), ()))
    contract_rows = (((0,), (0,)), ((), ()))
    gate_part = jnp.dot(rows_all, gate_weight, preferred_element_type=jnp.float32)
    up_part = jnp.dot(rows_all, up_weight, preferred_element_type=jnp.float32)
    grad_part = lax.dot_general(
        grads_all, down_weight, contract_cols, preferred_element_type=jnp.float32
    )
    hid = gate_part.shape[1]
    chunk = n_tok // n_col
    parts = jnp.stack([p.reshape(n_col, chunk, hid) for p in (gate_part, up_part, grad_part)], axis=1)
    parts = with_layout_constraint(parts, Layout(major_to_minor=(0, 1, 2, 3)))
    parts = lax.all_to_all(parts, "col", 0, 0, tiled=True)
    groups = parts.reshape((4, n_col // 4) + parts.shape[1:]).sum(axis=1)
    gate, up, hidden_grad = lax.optimization_barrier(groups).sum(axis=0)
    small = jnp.stack(pointwise(gate, up, hidden_grad))
    spread = jnp.broadcast_to(small[None], (n_col,) + small.shape)
    spread = lax.all_to_all(spread, "col", 0, 0, tiled=True)
    spread = spread.transpose(1, 0, 2, 3).reshape(3, n_tok, hid)
    hidden, gate_grad, up_grad = spread[0], spread[1], spread[2]
    gate_weight_grad = lax.dot_general(
        rows_all, gate_grad, contract_rows, preferred_element_type=jnp.float32
    ).astype(jnp.bfloat16)
    up_weight_grad = lax.dot_general(
        rows_all, up_grad, contract_rows, preferred_element_type=jnp.float32
    ).astype(jnp.bfloat16)
    down_weight_grad = lax.dot_general(
        hidden, grads_all, contract_rows, preferred_element_type=jnp.float32
    ).astype(jnp.bfloat16)
    total = lax.dot_general(
        gate_grad, gate_weight, contract_cols, preferred_element_type=jnp.float32
    ) + lax.dot_general(up_grad, up_weight, contract_cols, preferred_element_type=jnp.float32)
    block = n_tok // (n_z * n_core)
    total = total.reshape(n_z, n_core, block, width).transpose(1, 0, 2, 3)
    total = lax.all_to_all(total, "core", 0, 0, tiled=True)
    total = total[0] + total[1]
    input_grad = lax.all_to_all(total, "z", 0, 0, tiled=True).sum(axis=0)
    return (input_grad.astype(jnp.bfloat16), gate_weight_grad, up_weight_grad, down_weight_grad)


def solution(mesh):
    n_row, n_col = mesh.shape["row"], mesh.shape["col"]
    split = Mesh(mesh.devices.reshape(n_row // 2, 2, n_col), ("z", "core", "col"))
    return jax.shard_map(
        body,
        mesh=split,
        in_specs=(
            P(ROW, "col"),
            P(ROW, "col"),
            P("col", ROW),
            P("col", ROW),
            P(ROW, "col"),
        ),
        out_specs=(P(ROW, "col"), P("col", ROW), P("col", ROW), P(ROW, "col")),
        check_vma=False,
    )
```

```python
import jax
import jax.numpy as jnp
from jax import lax
from jax.experimental.layout import Layout, with_layout_constraint
from jax.sharding import Mesh, PartitionSpec as P

ROW = ("z", "core")


def pointwise(gate, up, hidden_grad):
    sig = jax.nn.sigmoid(gate)
    act = gate * sig
    hidden = (act * up).astype(jnp.bfloat16)
    gate_grad = (hidden_grad * up * sig * (1.0 + gate * (1.0 - sig))).astype(jnp.bfloat16)
    up_grad = (hidden_grad * act).astype(jnp.bfloat16)
    return (hidden, gate_grad, up_grad)


def gather_rows(tokens, out_grad, n_z, n_core):
    both = jnp.stack([tokens, out_grad])
    both = jnp.broadcast_to(both[None], (n_z,) + both.shape)
    both = both.reshape((n_z * n_core,) + tokens.shape)
    mine = lax.all_to_all(both, ROW, 0, 0, tiled=True)
    mine = mine.reshape((1, -1) + tokens.shape[1:])
    mine = jnp.broadcast_to(mine, (n_core,) + mine.shape[1:])
    full = lax.all_to_all(mine, "core", 0, 0, tiled=True)
    return full[0], full[1]


def body(tokens, out_grad, gate_weight, up_weight, down_weight):
    n_col = lax.psum(1, "col")
    n_z = lax.psum(1, "z")
    n_core = lax.psum(1, "core")
    rows_all, grads_all = gather_rows(tokens, out_grad, n_z, n_core)
    n_tok, width = rows_all.shape
    contract_cols = (((1,), (1,)), ((), ()))
    contract_rows = (((0,), (0,)), ((), ()))
    gate_part = jnp.dot(rows_all, gate_weight, preferred_element_type=jnp.float32)
    up_part = jnp.dot(rows_all, up_weight, preferred_element_type=jnp.float32)
    grad_part = lax.dot_general(
        grads_all, down_weight, contract_cols, preferred_element_type=jnp.float32
    )
    hid = gate_part.shape[1]
    chunk = n_tok // n_col
    parts = jnp.stack([p.reshape(n_col, chunk, hid) for p in (gate_part, up_part, grad_part)], axis=1)
    parts = with_layout_constraint(parts, Layout(major_to_minor=(0, 1, 2, 3)))
    parts = lax.all_to_all(parts, "col", 0, 0, tiled=True)
    groups = parts.reshape((4, n_col // 4) + parts.shape[1:]).sum(axis=1)
    gate, up, hidden_grad = lax.optimization_barrier(groups).sum(axis=0)
    small = jnp.concatenate(pointwise(gate, up, hidden_grad), axis=1)
    spread = jnp.broadcast_to(small[None], (n_col,) + small.shape)
    spread = lax.all_to_all(spread, "col", 0, 0, tiled=True).reshape(n_tok, 3 * hid)
    hidden, gate_grad, up_grad = spread[:, :hid], spread[:, hid:2 * hid], spread[:, 2 * hid:]
    gate_weight_grad = lax.dot_general(
        rows_all, gate_grad, contract_rows, preferred_element_type=jnp.float32
    ).astype(jnp.bfloat16)
    up_weight_grad = lax.dot_general(
        rows_all, up_grad, contract_rows, preferred_element_type=jnp.float32
    ).astype(jnp.bfloat16)
    down_weight_grad = lax.dot_general(
        hidden, grads_all, contract_rows, preferred_element_type=jnp.float32
    ).astype(jnp.bfloat16)
    total = lax.dot_general(
        gate_grad, gate_weight, contract_cols, preferred_element_type=jnp.float32
    ) + lax.dot_general(up_grad, up_weight, contract_cols, preferred_element_type=jnp.float32)
    block = n_tok // (n_z * n_core)
    total = total.reshape(n_z, n_core, block, width).transpose(1, 0, 2, 3)
    total = lax.all_to_all(total, "core", 0, 0, tiled=True)
    total = total[0] + total[1]
    input_grad = lax.all_to_all(total, "z", 0, 0, tiled=True).sum(axis=0)
    return (input_grad.astype(jnp.bfloat16), gate_weight_grad, up_weight_grad, down_weight_grad)


def solution(mesh):
    n_row, n_col = mesh.shape["row"], mesh.shape["col"]
    split = Mesh(mesh.devices.reshape(n_row // 2, 2, n_col), ("z", "core", "col"))
    return jax.shard_map(
        body,
        mesh=split,
        in_specs=(
            P(ROW, "col"),
            P(ROW, "col"),
            P("col", ROW),
            P("col", ROW),
            P(ROW, "col"),
        ),
        out_specs=(P(ROW, "col"), P("col", ROW), P("col", ROW), P(ROW, "col")),
        check_vma=False,
    )
```

```python
import jax
import jax.numpy as jnp
from jax import lax
from jax.experimental.layout import Layout, with_layout_constraint
from jax.sharding import Mesh, PartitionSpec as P

ROW = ("z", "core")


def pointwise(gate, up, hidden_grad):
    sig = jax.nn.sigmoid(gate)
    act = gate * sig
    hidden = (act * up).astype(jnp.bfloat16)
    gate_grad = (hidden_grad * up * sig * (1.0 + gate * (1.0 - sig))).astype(jnp.bfloat16)
    up_grad = (hidden_grad * act).astype(jnp.bfloat16)
    return (hidden, gate_grad, up_grad)


def gather_rows(tokens, out_grad, n_z, n_core):
    shape = (n_z, n_core) + tokens.shape
    to_core = lax.broadcasted_iota(jnp.int32, shape, 1)
    both = jnp.where(to_core == 0, jnp.broadcast_to(tokens, shape), jnp.broadcast_to(out_grad, shape))
    both = both.reshape((n_z * n_core,) + tokens.shape)
    mine = lax.all_to_all(both, ROW, 0, 0, tiled=True)
    mine = mine.reshape((1, -1) + tokens.shape[1:])
    mine = jnp.broadcast_to(mine, (n_core,) + mine.shape[1:])
    full = lax.all_to_all(mine, "core", 0, 0, tiled=True)
    return full[0], full[1]


def body(tokens, out_grad, gate_weight, up_weight, down_weight):
    n_col = lax.psum(1, "col")
    n_z = lax.psum(1, "z")
    n_core = lax.psum(1, "core")
    rows_all, grads_all = gather_rows(tokens, out_grad, n_z, n_core)
    n_tok, width = rows_all.shape
    contract_cols = (((1,), (1,)), ((), ()))
    contract_rows = (((0,), (0,)), ((), ()))
    gate_part = jnp.dot(rows_all, gate_weight, preferred_element_type=jnp.float32)
    up_part = jnp.dot(rows_all, up_weight, preferred_element_type=jnp.float32)
    grad_part = lax.dot_general(
        grads_all, down_weight, contract_cols, preferred_element_type=jnp.float32
    )
    hid = gate_part.shape[1]
    chunk = n_tok // n_col
    parts = jnp.stack([p.reshape(n_col, chunk, hid) for p in (gate_part, up_part, grad_part)], axis=1)
    parts = with_layout_constraint(parts, Layout(major_to_minor=(0, 1, 2, 3)))
    parts = lax.all_to_all(parts, "col", 0, 0, tiled=True)
    groups = parts.reshape((4, n_col // 4) + parts.shape[1:]).sum(axis=1)
    gate, up, hidden_grad = lax.optimization_barrier(groups).sum(axis=0)
    small = jnp.stack(pointwise(gate, up, hidden_grad))
    spread = jnp.broadcast_to(small[None], (n_col,) + small.shape)
    spread = lax.all_to_all(spread, "col", 0, 0, tiled=True)
    spread = spread.transpose(1, 0, 2, 3).reshape(3, n_tok, hid)
    hidden, gate_grad, up_grad = spread[0], spread[1], spread[2]
    gate_weight_grad = lax.dot_general(
        rows_all, gate_grad, contract_rows, preferred_element_type=jnp.float32
    ).astype(jnp.bfloat16)
    up_weight_grad = lax.dot_general(
        rows_all, up_grad, contract_rows, preferred_element_type=jnp.float32
    ).astype(jnp.bfloat16)
    down_weight_grad = lax.dot_general(
        hidden, grads_all, contract_rows, preferred_element_type=jnp.float32
    ).astype(jnp.bfloat16)
    total = lax.dot_general(
        gate_grad, gate_weight, contract_cols, preferred_element_type=jnp.float32
    ) + lax.dot_general(up_grad, up_weight, contract_cols, preferred_element_type=jnp.float32)
    block = n_tok // (n_z * n_core)
    total = total.reshape(n_z, n_core, block, width).transpose(1, 0, 2, 3)
    total = lax.all_to_all(total, "core", 0, 0, tiled=True)
    total = total[0] + total[1]
    input_grad = lax.all_to_all(total, "z", 0, 0, tiled=True).sum(axis=0)
    return (input_grad.astype(jnp.bfloat16), gate_weight_grad, up_weight_grad, down_weight_grad)


def solution(mesh):
    n_row, n_col = mesh.shape["row"], mesh.shape["col"]
    split = Mesh(mesh.devices.reshape(n_row // 2, 2, n_col), ("z", "core", "col"))
    return jax.shard_map(
        body,
        mesh=split,
        in_specs=(
            P(ROW, "col"),
            P(ROW, "col"),
            P("col", ROW),
            P("col", ROW),
            P(ROW, "col"),
        ),
        out_specs=(P(ROW, "col"), P("col", ROW), P("col", ROW), P(ROW, "col")),
        check_vma=False,
    )
```
